128 devices in a mesh: rows: 32 (over y, z, x_lo), chan: 4 (over x_hi, core).
Axes of the slice: x: 4 (x_hi: 2, x_lo: 2; x = x_hi * 2 + x_lo), y: 4, z: 4, core: 2. Of those that a mesh axis runs over, the one named last changes fastest.
Arguments:
- latent: bfloat16 [128, 128, 1280], P('rows', None, 'chan'), may hold values from -6 to 6
- stale_latent: bfloat16 [64, 128, 1280], P('rows', None, 'chan'), may hold values from -6 to 6
- stale_hidden: bfloat16 [64, 128, 1280], P('rows', None, 'chan'), may hold values from -4 to 4
- first_kernel: bfloat16 [3, 3, 1280, 1280], P(None, None, None, 'chan'), may hold values from -0.0546875 to 0.0546875
- second_kernel: bfloat16 [3, 3, 1280, 1280], P(None, None, None, 'chan'), may hold values from -0.0546875 to 0.0546875
- scale_table: float32 [1000, 1280], P(None, 'chan'), may hold values from 0.3 to 3
- timestep: int32 [1], replicated, may hold values from 0 to 999
- cotangent: bfloat16 [128, 128, 1280], P('rows', None, 'chan'), may hold values from -6 to 6
Outputs:
- output: bfloat16 [128, 128, 1280], P('rows', None, 'chan')
- grad_latent: bfloat16 [128, 128, 1280], P('rows', None, 'chan')
- grad_first: float32 [3, 3, 1280, 1280], P(None, None, 'rows', 'chan')
- grad_second: float32 [3, 3, 1280, 1280], P(None, None, 'rows', 'chan')
The draws below stay inside these ranges and needn't reach their ends.
Inputs may be any that keep to these rules, and one draw needn't show every extreme that they name: `timestep`: selects a row of scale_table.
All inputs are finite; a program needn't handle non-finite values.
Results may differ from the reference program's by a relative error of at most 0.0058.
Values may be sent and summed in bfloat16 or wider, within the bound.
No kernel may reach another device: no remote copies, remote signals or barrier semaphores. Data moves between devices by JAX's collectives and lax.ppermute only.
A program may use at most 192 MiB of HBM per device.

```python
import math
import jax
import jax.numpy as jnp
from jax import lax

C = 1280
W = 128
ROWS_DEV = 4
STEPS = 1000
H = 128
N_ROWS = 32


def strengthened(entries, key, source, target, parts, factor):
    owner, partner = [(jnp.arange(entries.shape[dim]) // (entries.shape[dim] // parts)).reshape([-1 if axis == dim else 1 for axis in range(entries.ndim)]) for dim in (source, target)]
    chosen = jax.random.permutation(key, parts)[partner]
    strong = (owner == chosen) | (owner == (partner + parts // 2) % parts)
    return jnp.where(strong, factor * entries, entries)


def block_levels(rng, extent, split, least, largest):
    def one(axis_at, parts):
        draws = jax.random.uniform(jax.random.fold_in(jax.random.fold_in(rng, 6), axis_at), (parts,), jnp.float32, least / len(split), largest / len(split))
        return jnp.repeat(jnp.exp(draws), extent[axis_at] // parts).reshape((-1,) + (1,) * (len(extent) - axis_at - 1))

    loudness = one(*split[0])
    for cut in split[1:]:
        loudness = loudness * one(*cut)
    return loudness


def bell_draw(stream_key, extent, scale, limit, shards=(), kind=jnp.bfloat16):
    values = jax.random.normal(stream_key, extent, jnp.float32) * scale
    if len(shards) > 0:
        values = block_levels(stream_key, extent, shards, -0.22, 0.18) * values
    return jnp.clip(values, min=-limit, max=limit).astype(kind)


def heavy_noise(stream_key, extent, scale, bound, split, heavy, dtype=jnp.bfloat16):
    entries = scale * jax.random.normal(stream_key, extent, jnp.float32)
    if split:
        entries = entries * block_levels(stream_key, extent, split, -0.22, 0.18)
    return jnp.clip(strengthened(entries, jax.random.fold_in(stream_key, 3), *heavy), -bound, bound).astype(dtype)


def setup_inputs(seed: int = 0) -> dict:
    key_list = jax.random.split(jax.random.key(seed), 9)
    latent = heavy_noise(key_list[0], (H, W, C), 1.0, 6.0, ((0, 32), (2, 4)), (0, 2, 32, 2.75))
    stale_latent = bell_draw(key_list[1], (2 * N_ROWS, W, C), 1.0, 6.0, ((0, 32), (2, 4)))
    stale_hidden = bell_draw(key_list[2], (2 * N_ROWS, W, C), 0.6, 4.0, ((0, 32), (2, 4)))
    first_kernel = bell_draw(key_list[3], (3, 3, C, C), (9 * C) ** -0.5, 0.0546875, ((3, 4),))
    second_kernel = bell_draw(key_list[4], (3, 3, C, C), (9 * C) ** -0.5, 0.0546875, ((3, 4),))
    scale_table = jnp.clip(jnp.exp(math.log(3.0) - 2.3025851 * jax.random.uniform(key_list[5], (STEPS, C), jnp.float32) ** block_levels(key_list[5], (STEPS, C), ((1, 4),), -0.2, 0.2)), 0.3, 3.0)
    timestep = jax.random.randint(key_list[6], (1,), 0, STEPS).astype(jnp.int32)
    cotangent = bell_draw(key_list[7], (H, W, C), 1.0, 6.0, ((0, 32), (2, 4)))
    return dict(latent=latent, stale_latent=stale_latent, stale_hidden=stale_hidden, first_kernel=first_kernel, second_kernel=second_kernel, scale_table=scale_table, timestep=timestep, cotangent=cotangent)


def silu_slope(values):
    logistic = jax.nn.sigmoid(values)
    return logistic * (1.0 + values * (1.0 - logistic))


def conv_rows(padded, kernel):
    result = lax.conv_general_dilated(padded[None].astype(jnp.float32), kernel.astype(jnp.float32), (1, 1), ((0, 0), (1, 1)), dimension_numbers=("NHWC", "HWIO", "NHWC"), precision=lax.Precision.HIGHEST)
    return result[0]


def flipped(kernel):
    return jnp.transpose(kernel[::-1, ::-1], (0, 1, 3, 2))


def stale_blocks(field, edges):
    block_rows = field.reshape(N_ROWS, ROWS_DEV, W, C)
    edge_rows = edges.reshape(N_ROWS, 2, W, C)
    position = jnp.arange(N_ROWS)[:, None, None]
    above = jnp.where(position > 0, edge_rows[:, 0], jnp.zeros_like(edge_rows[:, 0]))
    below = jnp.where(position < N_ROWS - 1, edge_rows[:, 1], jnp.zeros_like(edge_rows[:, 1]))
    return jnp.concatenate([above[:, None], block_rows, below[:, None]], axis=1)


def tap_sums(padded, grads):
    row_count, col_count, out_width = grads.shape
    flat_grads = grads.reshape(row_count * col_count, out_width).astype(jnp.float32)
    pieces = []
    for row_tap in range(3):
        for col_tap in range(3):
            window = padded[row_tap:row_tap + row_count, col_tap:col_tap + col_count]
            window = window.reshape(row_count * col_count, -1).astype(jnp.float32)
            pieces.append(lax.dot_general(window, flat_grads, (((0,), (0,)), ((), ())), precision=lax.Precision.HIGHEST))
    stacked = jnp.stack(pieces)
    return stacked.reshape(3, 3, stacked.shape[1], out_width)


def reference(latent, stale_latent, stale_hidden, first_kernel, second_kernel, scale_table, timestep, cotangent):
    latent_f = latent.astype(jnp.float32)
    act = jax.nn.silu(latent_f).astype(jnp.bfloat16)
    edge_act = jax.nn.silu(stale_latent.astype(jnp.float32)).astype(jnp.bfloat16)
    pre_act = lax.map(lambda padded: conv_rows(padded, first_kernel), stale_blocks(act, edge_act)).reshape(H, W, C)
    step_scale = jnp.sum(jnp.where(jnp.arange(STEPS)[:, None] == timestep[0], scale_table, 0.0), axis=0)
    scaled = pre_act * step_scale
    hidden = jax.nn.silu(scaled).astype(jnp.bfloat16)
    second = lax.map(lambda padded: conv_rows(padded, second_kernel), stale_blocks(hidden, stale_hidden)).reshape(H, W, C)
    output = (latent_f + second).astype(jnp.bfloat16)
    row_pad = ((1, 1), (0, 0), (0, 0))
    grad_hidden = conv_rows(jnp.pad(cotangent, row_pad), flipped(second_kernel))
    delta = (grad_hidden * silu_slope(scaled) * step_scale).astype(jnp.bfloat16)
    grad_pre = conv_rows(jnp.pad(delta, row_pad), flipped(first_kernel))
    grad_latent = (latent_f * 0.0 + cotangent.astype(jnp.float32) + grad_pre * silu_slope(latent_f)).astype(jnp.bfloat16)
    border = ((1, 1), (1, 1), (0, 0))
    grad_second = tap_sums(jnp.pad(hidden, border), cotangent) / H
    grad_first = tap_sums(jnp.pad(act, border), delta) / H
    return output, grad_latent, grad_first, grad_second
```

```python
import jax
import jax.numpy as jnp
from jax import lax
from jax.sharding import Mesh
from jax.sharding import PartitionSpec as P

ROWS = ("ry", "rk")


def extended(shard, axis, peers, dim, width):
    length = shard.shape[dim]
    up = [(i, (i + 1) % peers) for i in range(peers - 1)]
    down = [(j, i) for i, j in up]
    last = lax.slice_in_dim(shard, length - width, length, axis=dim)
    leading = lax.slice_in_dim(shard, 0, width, axis=dim)
    before = lax.ppermute(last, axis, up)
    after = lax.ppermute(leading, axis, down)
    return jnp.concatenate([before, shard, after], axis=dim)


def silu_slope(values):
    logistic = jax.nn.sigmoid(values)
    return logistic * (1.0 + values * (1.0 - logistic))


def conv_rows(padded, kernel):
    result = lax.conv_general_dilated(
        padded[None],
        kernel,
        (1, 1),
        ((0, 0), (1, 1)),
        dimension_numbers=("NHWC", "HWIO", "NHWC"),
        preferred_element_type=jnp.float32,
    )
    return result[0]


def flipped(kernel):
    return jnp.transpose(kernel[::-1, ::-1], (0, 1, 3, 2))


def weight_grad(field_ext, grads, groups):
    rows, cols, out_width = grads.shape
    width = field_ext.shape[2] // groups
    pieces = field_ext.reshape(rows + 2, cols, groups, width).transpose(2, 0, 1, 3)
    fields = lax.all_to_all(pieces, "ry", 0, 0, tiled=True)
    fields = jnp.pad(fields, ((0, 0), (0, 0), (1, 1), (0, 0)))
    grads_all = lax.all_gather(grads, "ry", axis=0, tiled=False)
    flat_grads = grads_all.reshape(groups * rows * cols, out_width)
    taps = []
    for row_tap in range(3):
        for col_tap in range(3):
            window = fields[:, row_tap : row_tap + rows, col_tap : col_tap + cols]
            window = window.reshape(groups * rows * cols, width)
            taps.append(
                lax.dot_general(
                    window, flat_grads, (((0,), (0,)), ((), ())), preferred_element_type=jnp.float32
                )
            )
    partial = jnp.stack(taps).reshape(3, 3, width, out_width)
    return lax.psum_scatter(partial, "rk", scatter_dimension=2, tiled=True)


def make_body(groups, row_devices):
    def on_device(
        latent,
        stale_latent,
        stale_hidden,
        first_kernel,
        second_kernel,
        scale_table,
        timestep,
        cotangent,
    ):
        row_index = lax.axis_index(ROWS)
        height = latent.shape[0] * row_devices
        latent_f = latent.astype(jnp.float32)
        act = jax.nn.silu(latent_f).astype(jnp.bfloat16)
        edge_act = jax.nn.silu(stale_latent.astype(jnp.float32)).astype(jnp.bfloat16)
        act_all, edge_all = (
            lax.all_gather(act, "chan", axis=2, tiled=True),
            lax.all_gather(edge_act, "chan", axis=2, tiled=True),
        )

        def stale_pad(field, edges):
            above = jnp.where(row_index > 0, edges[0], jnp.zeros_like(edges[0]))
            below = jnp.where(row_index < row_devices - 1, edges[1], jnp.zeros_like(edges[1]))
            return jnp.concatenate([above[None], field, below[None]], axis=0)

        pre_act = conv_rows(stale_pad(act_all, edge_all), first_kernel)
        steps_iota = jnp.arange(scale_table.shape[0])[:, None]
        step_scale = jnp.sum(jnp.where(steps_iota == timestep[0], scale_table, 0.0), axis=0)
        scaled = pre_act * step_scale
        hidden = jax.nn.silu(scaled).astype(jnp.bfloat16)
        hidden_all, edge_hidden = (
            lax.all_gather(hidden, "chan", axis=2, tiled=True),
            lax.all_gather(stale_hidden, "chan", axis=2, tiled=True),
        )
        output = (latent_f + conv_rows(stale_pad(hidden_all, edge_hidden), second_kernel)).astype(
            jnp.bfloat16
        )
        grad_pad = extended(cotangent, ROWS, row_devices, 0, 1)
        grad_hidden = lax.psum_scatter(
            conv_rows(grad_pad, flipped(second_kernel)), "chan", scatter_dimension=2, tiled=True
        )
        delta = (grad_hidden * silu_slope(scaled) * step_scale).astype(jnp.bfloat16)
        delta_pad = extended(delta, ROWS, row_devices, 0, 1)
        grad_pre = lax.psum_scatter(
            conv_rows(delta_pad, flipped(first_kernel)), "chan", scatter_dimension=2, tiled=True
        )
        grad_latent = (
            latent_f * 0.0 + cotangent.astype(jnp.float32) + grad_pre * silu_slope(latent_f)
        ).astype(jnp.bfloat16)
        rim_fields = extended(jnp.stack((act_all, hidden_all)), ROWS, row_devices, 1, 1)
        grad_second = weight_grad(rim_fields[1], cotangent, groups) / height
        grad_first = weight_grad(rim_fields[0], delta, groups) / height
        return (output, grad_latent, grad_first, grad_second)

    return on_device


def solution(mesh):
    row_devices, chan_devices = mesh.devices.shape
    groups = 4
    sub = Mesh(mesh.devices.reshape(groups, row_devices // groups, chan_devices), ("ry", "rk", "chan"))
    rows_spec = P(ROWS, None, "chan")
    in_specs = (
        rows_spec,
        rows_spec,
        rows_spec,
        P(None, None, None, "chan"),
        P(None, None, None, "chan"),
        P(None, "chan"),
        P(),
        rows_spec,
    )
    out_specs = (
        rows_spec,
        rows_spec,
        P(None, None, ROWS, "chan"),
        P(None, None, ROWS, "chan"),
    )
    return jax.shard_map(
        make_body(groups, row_devices), mesh=sub, in_specs=in_specs, out_specs=out_specs, check_vma=False
    )
```

```python
import jax
import jax.numpy as jnp
from jax import lax
from jax.sharding import Mesh
from jax.sharding import PartitionSpec as P

ROWS = ("ry", "rk")


def extended(shard, axis, peers, dim, width):
    length = shard.shape[dim]
    up = [(i, (i + 1) % peers) for i in range(peers - 1)]
    down = [(j, i) for i, j in up]
    last = lax.slice_in_dim(shard, length - width, length, axis=dim)
    leading = lax.slice_in_dim(shard, 0, width, axis=dim)
    before = lax.ppermute(last, axis, up)
    after = lax.ppermute(leading, axis, down)
    return jnp.concatenate([before, shard, after], axis=dim)


def silu_slope(values):
    logistic = jax.nn.sigmoid(values)
    return logistic * (1.0 + values * (1.0 - logistic))


def conv_rows(padded, kernel):
    result = lax.conv_general_dilated(
        padded[None],
        kernel,
        (1, 1),
        ((0, 0), (1, 1)),
        dimension_numbers=("NHWC", "HWIO", "NHWC"),
        preferred_element_type=jnp.float32,
    )
    return result[0]


def flipped(kernel):
    return jnp.transpose(kernel[::-1, ::-1], (0, 1, 3, 2))


def reduce_chunks(chunks, axis):
    received = lax.all_to_all(chunks, axis, 0, 0, tiled=True)
    return jnp.sum(received, axis=0)


def weight_grad(field_ext, grads, groups):
    rows, cols, out_width = grads.shape
    width = field_ext.shape[2] // groups
    pieces = field_ext.reshape(rows + 2, cols, groups, width).transpose(2, 0, 1, 3)
    fields = lax.all_to_all(pieces, "ry", 0, 0, tiled=True)
    fields = jnp.pad(fields, ((0, 0), (0, 0), (1, 1), (0, 0)))
    grads_all = lax.all_gather(grads, "ry", axis=0, tiled=False)
    flat_grads = grads_all.reshape(groups * rows * cols, out_width)
    taps = []
    for row_tap in range(3):
        for col_tap in range(3):
            window = fields[:, row_tap : row_tap + rows, col_tap : col_tap + cols]
            window = window.reshape(groups * rows * cols, width)
            taps.append(
                lax.dot_general(
                    window, flat_grads, (((0,), (0,)), ((), ())), preferred_element_type=jnp.float32
                )
            )
    parts = lax.axis_size("rk")
    partial = jnp.stack([t.reshape(parts, width // parts, out_width) for t in taps], axis=1)
    return reduce_chunks(partial, "rk").reshape(3, 3, width // parts, out_width)


def make_body(groups, row_devices):
    def on_device(
        latent,
        stale_latent,
        stale_hidden,
        first_kernel,
        second_kernel,
        scale_table,
        timestep,
        cotangent,
    ):
        row_index = lax.axis_index(ROWS)
        height = latent.shape[0] * row_devices
        latent_f = latent.astype(jnp.float32)
        act = jax.nn.silu(latent_f).astype(jnp.bfloat16)
        edge_act = jax.nn.silu(stale_latent.astype(jnp.float32)).astype(jnp.bfloat16)
        def gathered(field, edges):
            joined = jnp.concatenate([edges[0:1], field, edges[1:2]], axis=0)
            joined = lax.all_gather(joined, "chan", axis=2, tiled=True)
            rows = field.shape[0]
            above = jnp.where(row_index > 0, joined[0:1], jnp.zeros_like(joined[0:1]))
            below = jnp.where(row_index < row_devices - 1, joined[rows + 1 :], jnp.zeros_like(joined[0:1]))
            middle = joined[1 : rows + 1]
            return middle, jnp.concatenate([above, middle, below], axis=0)

        def chan_reduce(values):
            rows, cols, width = values.shape
            parts = lax.axis_size("chan")
            chunks = values.reshape(rows, cols, parts, width // parts).transpose(2, 0, 1, 3)
            return reduce_chunks(chunks, "chan")

        act_all, act_pad = gathered(act, edge_act)
        pre_act = conv_rows(act_pad, first_kernel)
        steps_iota = jnp.arange(scale_table.shape[0])[:, None]
        step_scale = jnp.sum(jnp.where(steps_iota == timestep[0], scale_table, 0.0), axis=0)
        scaled = pre_act * step_scale
        hidden = jax.nn.silu(scaled).astype(jnp.bfloat16)
        hidden_all, hidden_pad = gathered(hidden, stale_hidden)
        output = (latent_f + conv_rows(hidden_pad, second_kernel)).astype(jnp.bfloat16)
        grad_pad = extended(cotangent, ROWS, row_devices, 0, 1)
        grad_hidden = chan_reduce(conv_rows(grad_pad, flipped(second_kernel)))
        delta = (grad_hidden * silu_slope(scaled) * step_scale).astype(jnp.bfloat16)
        delta_pad = extended(delta, ROWS, row_devices, 0, 1)
        grad_pre = chan_reduce(conv_rows(delta_pad, flipped(first_kernel)))
        grad_latent = (
            latent_f * 0.0 + cotangent.astype(jnp.float32) + grad_pre * silu_slope(latent_f)
        ).astype(jnp.bfloat16)
        rim_fields = extended(jnp.stack((act_all, hidden_all)), ROWS, row_devices, 1, 1)
        grad_second = weight_grad(rim_fields[1], cotangent, groups) / height
        grad_first = weight_grad(rim_fields[0], delta, groups) / height
        return (output, grad_latent, grad_first, grad_second)

    return on_device


def solution(mesh):
    row_devices, chan_devices = mesh.devices.shape
    groups = 4
    sub = Mesh(mesh.devices.reshape(groups, row_devices // groups, chan_devices), ("ry", "rk", "chan"))
    rows_spec = P(ROWS, None, "chan")
    in_specs = (
        rows_spec,
        rows_spec,
        rows_spec,
        P(None, None, None, "chan"),
        P(None, None, None, "chan"),
        P(None, "chan"),
        P(),
        rows_spec,
    )
    out_specs = (
        rows_spec,
        rows_spec,
        P(None, None, ROWS, "chan"),
        P(None, None, ROWS, "chan"),
    )
    return jax.shard_map(
        make_body(groups, row_devices), mesh=sub, in_specs=in_specs, out_specs=out_specs, check_vma=False
    )
```

```python
import jax
import jax.numpy as jnp
from jax import lax
from jax.sharding import Mesh
from jax.sharding import PartitionSpec as P

ROWS = ("ry", "rk")


def extended(shard, axis, peers, dim, width):
    length = shard.shape[dim]
    up = [(i, (i + 1) % peers) for i in range(peers - 1)]
    down = [(j, i) for i, j in up]
    last = lax.slice_in_dim(shard, length - width, length, axis=dim)
    leading = lax.slice_in_dim(shard, 0, width, axis=dim)
    before = lax.ppermute(last, axis, up)
    after = lax.ppermute(leading, axis, down)
    return jnp.concatenate([before, shard, after], axis=dim)


def silu_slope(values):
    logistic = jax.nn.sigmoid(values)
    return logistic * (1.0 + values * (1.0 - logistic))


def conv_rows(padded, kernel):
    result = lax.conv_general_dilated(
        padded[None],
        kernel,
        (1, 1),
        ((0, 0), (1, 1)),
        dimension_numbers=("NHWC", "HWIO", "NHWC"),
        preferred_element_type=jnp.float32,
    )
    return result[0]


def flipped(kernel):
    return jnp.transpose(kernel[::-1, ::-1], (0, 1, 3, 2))


def reduce_chunks(chunks, axis):
    received = lax.all_to_all(chunks, axis, 0, 0, tiled=True)
    return jnp.sum(received, axis=0)


def weight_grad(field_ext, grads, groups):
    rows, cols, out_width = grads.shape
    width = field_ext.shape[2] // groups
    pieces = field_ext.reshape(rows + 2, cols, groups, width).transpose(2, 0, 1, 3)
    fields = lax.all_to_all(pieces, "ry", 0, 0, tiled=True)
    fields = jnp.pad(fields, ((0, 0), (0, 0), (1, 1), (0, 0)))
    grads_all = lax.all_gather(grads, "ry", axis=0, tiled=False)
    partial = lax.conv_general_dilated(
        fields,
        grads_all,
        (1, 1),
        "VALID",
        dimension_numbers=("CHWN", "IHWO", "HWNC"),
        preferred_element_type=jnp.float32,
    )
    parts = lax.axis_size("rk")
    partial = partial.reshape(3, 3, parts, width // parts, out_width).transpose(2, 0, 1, 3, 4)
    return reduce_chunks(partial, "rk")


def make_body(groups, row_devices):
    def on_device(
        latent,
        stale_latent,
        stale_hidden,
        first_kernel,
        second_kernel,
        scale_table,
        timestep,
        cotangent,
    ):
        row_index = lax.axis_index(ROWS)
        height = latent.shape[0] * row_devices
        latent_f = latent.astype(jnp.float32)
        act = jax.nn.silu(latent_f).astype(jnp.bfloat16)
        edge_act = jax.nn.silu(stale_latent.astype(jnp.float32)).astype(jnp.bfloat16)
        def gathered(field, edges):
            joined = jnp.concatenate([edges[0:1], field, edges[1:2]], axis=0)
            joined = lax.all_gather(joined, "chan", axis=2, tiled=True)
            rows = field.shape[0]
            above = jnp.where(row_index > 0, joined[0:1], jnp.zeros_like(joined[0:1]))
            below = jnp.where(row_index < row_devices - 1, joined[rows + 1 :], jnp.zeros_like(joined[0:1]))
            middle = joined[1 : rows + 1]
            return middle, jnp.concatenate([above, middle, below], axis=0)

        def chan_reduce(values):
            rows, cols, width = values.shape
            parts = lax.axis_size("chan")
            chunks = values.reshape(rows, cols, parts, width // parts).transpose(2, 0, 1, 3)
            return reduce_chunks(chunks, "chan")

        act_all, act_pad = gathered(act, edge_act)
        pre_act = conv_rows(act_pad, first_kernel)
        steps_iota = jnp.arange(scale_table.shape[0])[:, None]
        step_scale = jnp.sum(jnp.where(steps_iota == timestep[0], scale_table, 0.0), axis=0)
        scaled = pre_act * step_scale
        hidden = jax.nn.silu(scaled).astype(jnp.bfloat16)
        hidden_all, hidden_pad = gathered(hidden, stale_hidden)
        output = (latent_f + conv_rows(hidden_pad, second_kernel)).astype(jnp.bfloat16)
        grad_pad = extended(cotangent, ROWS, row_devices, 0, 1)
        grad_hidden = chan_reduce(conv_rows(grad_pad, flipped(second_kernel)))
        delta = (grad_hidden * silu_slope(scaled) * step_scale).astype(jnp.bfloat16)
        delta_pad = extended(delta, ROWS, row_devices, 0, 1)
        grad_pre = chan_reduce(conv_rows(delta_pad, flipped(first_kernel)))
        grad_latent = (
            latent_f * 0.0 + cotangent.astype(jnp.float32) + grad_pre * silu_slope(latent_f)
        ).astype(jnp.bfloat16)
        rim_fields = extended(jnp.stack((act_all, hidden_all)), ROWS, row_devices, 1, 1)
        grad_second = weight_grad(rim_fields[1], cotangent, groups) / height
        grad_first = weight_grad(rim_fields[0], delta, groups) / height
        return (output, grad_latent, grad_first, grad_second)

    return on_device


def solution(mesh):
    row_devices, chan_devices = mesh.devices.shape
    groups = 4
    sub = Mesh(mesh.devices.reshape(groups, row_devices // groups, chan_devices), ("ry", "rk", "chan"))
    rows_spec = P(ROWS, None, "chan")
    in_specs = (
        rows_spec,
        rows_spec,
        rows_spec,
        P(None, None, None, "chan"),
        P(None, None, None, "chan"),
        P(None, "chan"),
        P(),
        rows_spec,
    )
    out_specs = (
        rows_spec,
        rows_spec,
        P(None, None, ROWS, "chan"),
        P(None, None, ROWS, "chan"),
    )
    return jax.shard_map(
        make_body(groups, row_devices), mesh=sub, in_specs=in_specs, out_specs=out_specs, check_vma=False
    )
```

```python
import jax
import jax.numpy as jnp
from jax import lax
from jax.sharding import Mesh
from jax.sharding import PartitionSpec as P

ROWS = ("ry", "rk")


def extended(shard, axis, peers, dim, width):
    length = shard.shape[dim]
    up = [(i, (i + 1) % peers) for i in range(peers - 1)]
    down = [(j, i) for i, j in up]
    last = lax.slice_in_dim(shard, length - width, length, axis=dim)
    leading = lax.slice_in_dim(shard, 0, width, axis=dim)
    before = lax.ppermute(last, axis, up)
    after = lax.ppermute(leading, axis, down)
    return jnp.concatenate([before, shard, after], axis=dim)


def silu_slope(values):
    logistic = jax.nn.sigmoid(values)
    return logistic * (1.0 + values * (1.0 - logistic))


def conv_rows(padded, kernel):
    result = lax.conv_general_dilated(
        padded[None],
        kernel,
        (1, 1),
        ((0, 0), (1, 1)),
        dimension_numbers=("NHWC", "HWIO", "NHWC"),
        preferred_element_type=jnp.float32,
    )
    return result[0]


def flipped(kernel):
    return jnp.transpose(kernel[::-1, ::-1], (0, 1, 3, 2))


def reduce_chunks(chunks, axis):
    received = lax.all_to_all(chunks.astype(jnp.bfloat16), axis, 0, 0, tiled=True)
    return jnp.sum(received.astype(jnp.float32), axis=0)


def weight_grad(field_ext, grads, groups):
    rows, cols, out_width = grads.shape
    width = field_ext.shape[2] // groups
    pieces = field_ext.reshape(rows + 2, cols, groups, width).transpose(2, 0, 1, 3)
    fields = lax.all_to_all(pieces, "ry", 0, 0, tiled=True)
    fields = jnp.pad(fields, ((0, 0), (0, 0), (1, 1), (0, 0)))
    grads_all = lax.all_gather(grads, "ry", axis=0, tiled=False)
    partial = lax.conv_general_dilated(
        fields,
        grads_all,
        (1, 1),
        "VALID",
        dimension_numbers=("CHWN", "IHWO", "HWNC"),
        preferred_element_type=jnp.float32,
    )
    parts = lax.axis_size("rk")
    partial = partial.reshape(3, 3, parts, width // parts, out_width).transpose(2, 0, 1, 3, 4)
    return reduce_chunks(partial, "rk")


def make_body(groups, row_devices):
    def on_device(
        latent,
        stale_latent,
        stale_hidden,
        first_kernel,
        second_kernel,
        scale_table,
        timestep,
        cotangent,
    ):
        row_index = lax.axis_index(ROWS)
        height = latent.shape[0] * row_devices
        latent_f = latent.astype(jnp.float32)
        act = jax.nn.silu(latent_f).astype(jnp.bfloat16)
        edge_act = jax.nn.silu(stale_latent.astype(jnp.float32)).astype(jnp.bfloat16)
        def gathered(field, edges):
            joined = jnp.concatenate([edges[0:1], field, edges[1:2]], axis=0)
            joined = lax.all_gather(joined, "chan", axis=2, tiled=True)
            rows = field.shape[0]
            above = jnp.where(row_index > 0, joined[0:1], jnp.zeros_like(joined[0:1]))
            below = jnp.where(row_index < row_devices - 1, joined[rows + 1 :], jnp.zeros_like(joined[0:1]))
            middle = joined[1 : rows + 1]
            return middle, jnp.concatenate([above, middle, below], axis=0)

        def chan_reduce(values):
            rows, cols, width = values.shape
            parts = lax.axis_size("chan")
            chunks = values.reshape(rows, cols, parts, width // parts).transpose(2, 0, 1, 3)
            return reduce_chunks(chunks, "chan")

        act_all, act_pad = gathered(act, edge_act)
        pre_act = conv_rows(act_pad, first_kernel)
        steps_iota = jnp.arange(scale_table.shape[0])[:, None]
        step_scale = jnp.sum(jnp.where(steps_iota == timestep[0], scale_table, 0.0), axis=0)
        scaled = pre_act * step_scale
        hidden = jax.nn.silu(scaled).astype(jnp.bfloat16)
        hidden_all, hidden_pad = gathered(hidden, stale_hidden)
        output = (latent_f + conv_rows(hidden_pad, second_kernel)).astype(jnp.bfloat16)
        grad_pad = extended(cotangent, ROWS, row_devices, 0, 1)
        grad_hidden = chan_reduce(conv_rows(grad_pad, flipped(second_kernel)))
        delta = (grad_hidden * silu_slope(scaled) * step_scale).astype(jnp.bfloat16)
        delta_pad = extended(delta, ROWS, row_devices, 0, 1)
        grad_pre = chan_reduce(conv_rows(delta_pad, flipped(first_kernel)))
        grad_latent = (
            latent_f * 0.0 + cotangent.astype(jnp.float32) + grad_pre * silu_slope(latent_f)
        ).astype(jnp.bfloat16)
        rim_fields = extended(jnp.stack((act_all, hidden_all)), ROWS, row_devices, 1, 1)
        grad_second = weight_grad(rim_fields[1], cotangent, groups) / height
        grad_first = weight_grad(rim_fields[0], delta, groups) / height
        return (output, grad_latent, grad_first, grad_second)

    return on_device


def solution(mesh):
    row_devices, chan_devices = mesh.devices.shape
    groups = 4
    sub = Mesh(mesh.devices.reshape(groups, row_devices // groups, chan_devices), ("ry", "rk", "chan"))
    rows_spec = P(ROWS, None, "chan")
    in_specs = (
        rows_spec,
        rows_spec,
        rows_spec,
        P(None, None, None, "chan"),
        P(None, None, None, "chan"),
        P(None, "chan"),
        P(),
        rows_spec,
    )
    out_specs = (
        rows_spec,
        rows_spec,
        P(None, None, ROWS, "chan"),
        P(None, None, ROWS, "chan"),
    )
    return jax.shard_map(
        make_body(groups, row_devices), mesh=sub, in_specs=in_specs, out_specs=out_specs, check_vma=False
    )
```

```python
import jax
import jax.numpy as jnp
from jax import lax
from jax.sharding import Mesh
from jax.sharding import PartitionSpec as P

ROWS = ("ry", "rk")
CHAN = ("cx", "cc")


def extended(shard, axis, peers, dim, width):
    length = shard.shape[dim]
    up = [(i, (i + 1) % peers) for i in range(peers - 1)]
    down = [(j, i) for i, j in up]
    last = lax.slice_in_dim(shard, length - width, length, axis=dim)
    leading = lax.slice_in_dim(shard, 0, width, axis=dim)
    before = lax.ppermute(last, axis, up)
    after = lax.ppermute(leading, axis, down)
    return jnp.concatenate([before, shard, after], axis=dim)


def silu_slope(values):
    logistic = jax.nn.sigmoid(values)
    return logistic * (1.0 + values * (1.0 - logistic))


def conv_rows(padded, kernel):
    result = lax.conv_general_dilated(
        padded[None],
        kernel,
        (1, 1),
        ((0, 0), (1, 1)),
        dimension_numbers=("NHWC", "HWIO", "NHWC"),
        preferred_element_type=jnp.float32,
    )
    return result[0]


def flipped(kernel):
    return jnp.transpose(kernel[::-1, ::-1], (0, 1, 3, 2))


def reduce_chunks(chunks, axis, link_type=jnp.float32):
    received = lax.all_to_all(chunks.astype(link_type), axis, 0, 0, tiled=True)
    return jnp.sum(received.astype(jnp.float32), axis=0)


def weight_grad(field_ext, grads, groups):
    rows, cols, out_width = grads.shape
    width = field_ext.shape[2] // groups
    pieces = field_ext.reshape(rows + 2, cols, groups, width).transpose(2, 0, 1, 3)
    fields = lax.all_to_all(pieces, "ry", 0, 0, tiled=True)
    fields = jnp.pad(fields, ((0, 0), (0, 0), (1, 1), (0, 0)))
    grads_all = lax.all_gather(grads, "ry", axis=0, tiled=False)
    partial = lax.conv_general_dilated(
        fields,
        grads_all,
        (1, 1),
        "VALID",
        dimension_numbers=("CHWN", "IHWO", "HWNC"),
        preferred_element_type=jnp.float32,
    )
    parts = lax.axis_size("rk")
    partial = partial.reshape(3, 3, parts, width // parts, out_width).transpose(2, 0, 1, 3, 4)
    return reduce_chunks(partial, "rk", jnp.bfloat16)


def make_body(groups, row_devices):
    def on_device(
        latent,
        stale_latent,
        stale_hidden,
        first_kernel,
        second_kernel,
        scale_table,
        timestep,
        cotangent,
    ):
        row_index = lax.axis_index(ROWS)
        height = latent.shape[0] * row_devices
        latent_f = latent.astype(jnp.float32)
        act = jax.nn.silu(latent_f).astype(jnp.bfloat16)
        edge_act = jax.nn.silu(stale_latent.astype(jnp.float32)).astype(jnp.bfloat16)
        def gathered(field, edges):
            joined = jnp.concatenate([edges[0:1], field, edges[1:2]], axis=0)
            joined = lax.all_gather(joined, CHAN, axis=2, tiled=True)
            rows = field.shape[0]
            above = jnp.where(row_index > 0, joined[0:1], jnp.zeros_like(joined[0:1]))
            below = jnp.where(row_index < row_devices - 1, joined[rows + 1 :], jnp.zeros_like(joined[0:1]))
            middle = joined[1 : rows + 1]
            return middle, jnp.concatenate([above, middle, below], axis=0)

        def chan_reduce(values):
            rows, cols, width = values.shape
            outer, inner = lax.axis_size("cx"), lax.axis_size("cc")
            chunks = values.reshape(rows, cols, outer, inner, width // (outer * inner))
            chunks = chunks.transpose(3, 2, 0, 1, 4)
            return reduce_chunks(reduce_chunks(chunks, "cc"), "cx")

        act_all, act_pad = gathered(act, edge_act)
        pre_act = conv_rows(act_pad, first_kernel)
        steps_iota = jnp.arange(scale_table.shape[0])[:, None]
        step_scale = jnp.sum(jnp.where(steps_iota == timestep[0], scale_table, 0.0), axis=0)
        scaled = pre_act * step_scale
        hidden = jax.nn.silu(scaled).astype(jnp.bfloat16)
        hidden_all, hidden_pad = gathered(hidden, stale_hidden)
        output = (latent_f + conv_rows(hidden_pad, second_kernel)).astype(jnp.bfloat16)
        grad_pad = extended(cotangent, ROWS, row_devices, 0, 1)
        grad_hidden = chan_reduce(conv_rows(grad_pad, flipped(second_kernel)))
        delta = (grad_hidden * silu_slope(scaled) * step_scale).astype(jnp.bfloat16)
        delta_pad = extended(delta, ROWS, row_devices, 0, 1)
        grad_pre = chan_reduce(conv_rows(delta_pad, flipped(first_kernel)))
        grad_latent = (
            latent_f * 0.0 + cotangent.astype(jnp.float32) + grad_pre * silu_slope(latent_f)
        ).astype(jnp.bfloat16)
        rim_fields = extended(jnp.stack((act_all, hidden_all)), ROWS, row_devices, 1, 1)
        grad_second = weight_grad(rim_fields[1], cotangent, groups) / height
        grad_first = weight_grad(rim_fields[0], delta, groups) / height
        return (output, grad_latent, grad_first, grad_second)

    return on_device


def solution(mesh):
    row_devices, chan_devices = mesh.devices.shape
    groups = 4
    sub = Mesh(
        mesh.devices.reshape(groups, row_devices // groups, 2, chan_devices // 2), ("ry", "rk", "cx", "cc")
    )
    rows_spec = P(ROWS, None, CHAN)
    in_specs = (
        rows_spec,
        rows_spec,
        rows_spec,
        P(None, None, None, CHAN),
        P(None, None, None, CHAN),
        P(None, CHAN),
        P(),
        rows_spec,
    )
    out_specs = (
        rows_spec,
        rows_spec,
        P(None, None, ROWS, CHAN),
        P(None, None, ROWS, CHAN),
    )
    return jax.shard_map(
        make_body(groups, row_devices), mesh=sub, in_specs=in_specs, out_specs=out_specs, check_vma=False
    )
```

```python
import jax
import jax.numpy as jnp
from jax import lax
from jax.sharding import Mesh
from jax.sharding import PartitionSpec as P

ROWS = ("ry", "rk")
CHAN = ("cx", "cc")


def extended(shard, axis, peers, dim, width):
    length = shard.shape[dim]
    up = [(i, (i + 1) % peers) for i in range(peers - 1)]
    down = [(j, i) for i, j in up]
    last = lax.slice_in_dim(shard, length - width, length, axis=dim)
    leading = lax.slice_in_dim(shard, 0, width, axis=dim)
    before = lax.ppermute(last, axis, up)
    after = lax.ppermute(leading, axis, down)
    return jnp.concatenate([before, shard, after], axis=dim)


def silu_slope(values):
    logistic = jax.nn.sigmoid(values)
    return logistic * (1.0 + values * (1.0 - logistic))


def conv_rows(padded, kernel):
    result = lax.conv_general_dilated(
        padded[None],
        kernel,
        (1, 1),
        ((0, 0), (1, 1)),
        dimension_numbers=("NHWC", "HWIO", "NHWC"),
        preferred_element_type=jnp.float32,
    )
    return result[0]


def flipped(kernel):
    return jnp.transpose(kernel[::-1, ::-1], (0, 1, 3, 2))


def reduce_chunks(chunks, axis, link_type=jnp.float32):
    received = lax.all_to_all(chunks.astype(link_type), axis, 0, 0, tiled=True)
    return jnp.sum(received.astype(jnp.float32), axis=0)


def weight_grad(field_ext, grads, groups):
    rows, cols, out_width = grads.shape
    width = field_ext.shape[2] // groups
    pieces = field_ext.reshape(rows + 2, cols, groups, width).transpose(2, 0, 1, 3)
    fields = lax.all_to_all(pieces, "ry", 0, 0, tiled=True)
    fields = jnp.pad(fields, ((0, 0), (0, 0), (1, 1), (0, 0)))
    grads_all = lax.all_to_all(jnp.broadcast_to(grads[None], (groups,) + grads.shape), "ry", 0, 0, tiled=True)
    partial = lax.conv_general_dilated(
        fields,
        grads_all,
        (1, 1),
        "VALID",
        dimension_numbers=("CHWN", "IHWO", "HWNC"),
        preferred_element_type=jnp.float32,
    )
    parts = lax.axis_size("rk")
    partial = partial.reshape(3, 3, parts, width // parts, out_width).transpose(2, 0, 1, 3, 4)
    return reduce_chunks(partial, "rk", jnp.bfloat16)


def make_body(groups, row_devices):
    def on_device(
        latent,
        stale_latent,
        stale_hidden,
        first_kernel,
        second_kernel,
        scale_table,
        timestep,
        cotangent,
    ):
        row_index = lax.axis_index(ROWS)
        height = latent.shape[0] * row_devices
        latent_f = latent.astype(jnp.float32)
        act = jax.nn.silu(latent_f).astype(jnp.bfloat16)
        edge_act = jax.nn.silu(stale_latent.astype(jnp.float32)).astype(jnp.bfloat16)
        def gathered(field, edges):
            joined = jnp.concatenate([edges[0:1], field, edges[1:2]], axis=0)
            joined = lax.all_gather(joined, CHAN, axis=2, tiled=True)
            rows = field.shape[0]
            above = jnp.where(row_index > 0, joined[0:1], jnp.zeros_like(joined[0:1]))
            below = jnp.where(row_index < row_devices - 1, joined[rows + 1 :], jnp.zeros_like(joined[0:1]))
            middle = joined[1 : rows + 1]
            return middle, jnp.concatenate([above, middle, below], axis=0)

        def chan_reduce(values):
            rows, cols, width = values.shape
            outer, inner = lax.axis_size("cx"), lax.axis_size("cc")
            chunks = values.reshape(rows, cols, outer, inner, width // (outer * inner))
            chunks = chunks.transpose(3, 2, 0, 1, 4)
            return reduce_chunks(reduce_chunks(chunks, "cc"), "cx")

        act_all, act_pad = gathered(act, edge_act)
        pre_act = conv_rows(act_pad, first_kernel)
        steps_iota = jnp.arange(scale_table.shape[0])[:, None]
        step_scale = jnp.sum(jnp.where(steps_iota == timestep[0], scale_table, 0.0), axis=0)
        scaled = pre_act * step_scale
        hidden = jax.nn.silu(scaled).astype(jnp.bfloat16)
        hidden_all, hidden_pad = gathered(hidden, stale_hidden)
        output = (latent_f + conv_rows(hidden_pad, second_kernel)).astype(jnp.bfloat16)
        grad_pad = extended(cotangent, ROWS, row_devices, 0, 1)
        grad_hidden = chan_reduce(conv_rows(grad_pad, flipped(second_kernel)))
        delta = (grad_hidden * silu_slope(scaled) * step_scale).astype(jnp.bfloat16)
        delta_pad = extended(delta, ROWS, row_devices, 0, 1)
        grad_pre = chan_reduce(conv_rows(delta_pad, flipped(first_kernel)))
        grad_latent = (
            latent_f * 0.0 + cotangent.astype(jnp.float32) + grad_pre * silu_slope(latent_f)
        ).astype(jnp.bfloat16)
        rim_fields = extended(jnp.stack((act_all, hidden_all)), ROWS, row_devices, 1, 1)
        grad_second = weight_grad(rim_fields[1], cotangent, groups) / height
        grad_first = weight_grad(rim_fields[0], delta, groups) / height
        return (output, grad_latent, grad_first, grad_second)

    return on_device


def solution(mesh):
    row_devices, chan_devices = mesh.devices.shape
    groups = 4
    sub = Mesh(
        mesh.devices.reshape(groups, row_devices // groups, 2, chan_devices // 2), ("ry", "rk", "cx", "cc")
    )
    rows_spec = P(ROWS, None, CHAN)
    in_specs = (
        rows_spec,
        rows_spec,
        rows_spec,
        P(None, None, None, CHAN),
        P(None, None, None, CHAN),
        P(None, CHAN),
        P(),
        rows_spec,
    )
    out_specs = (
        rows_spec,
        rows_spec,
        P(None, None, ROWS, CHAN),
        P(None, None, ROWS, CHAN),
    )
    return jax.shard_map(
        make_body(groups, row_devices), mesh=sub, in_specs=in_specs, out_specs=out_specs, check_vma=False
    )
```

```python
import jax
import jax.numpy as jnp
from jax import lax
from jax.sharding import Mesh
from jax.sharding import PartitionSpec as P

ROWS = ("ry", "rk")
CHAN = ("cx", "cc")


def extended(shard, axis, peers, dim, width):
    length = shard.shape[dim]
    up = [(i, (i + 1) % peers) for i in range(peers - 1)]
    down = [(j, i) for i, j in up]
    last = lax.slice_in_dim(shard, length - width, length, axis=dim)
    leading = lax.slice_in_dim(shard, 0, width, axis=dim)
    before = lax.ppermute(last, axis, up)
    after = lax.ppermute(leading, axis, down)
    return jnp.concatenate([before, shard, after], axis=dim)


def silu_slope(values):
    logistic = jax.nn.sigmoid(values)
    return logistic * (1.0 + values * (1.0 - logistic))


def conv_rows(padded, kernel):
    result = lax.conv_general_dilated(
        padded[None],
        kernel,
        (1, 1),
        ((0, 0), (1, 1)),
        dimension_numbers=("NHWC", "HWIO", "NHWC"),
        preferred_element_type=jnp.float32,
    )
    return result[0]


def flipped(kernel):
    return jnp.transpose(kernel[::-1, ::-1], (0, 1, 3, 2))


def reduce_chunks(chunks, axis, link_type=jnp.float32):
    received = lax.all_to_all(chunks.astype(link_type), axis, 0, 0, tiled=True)
    return jnp.sum(received.astype(jnp.float32), axis=0)


def weight_grad(field_ext, grads, groups):
    rows, cols, out_width = grads.shape
    width = field_ext.shape[2] // groups
    pieces = field_ext.reshape(rows + 2, cols, groups, width).transpose(2, 0, 1, 3)
    fields = lax.all_to_all(pieces, "ry", 0, 0, tiled=True)
    fields = jnp.pad(fields, ((0, 0), (0, 0), (1, 1), (0, 0)))
    grads_all = lax.all_gather(grads, "ry", axis=0, tiled=False)
    partial = lax.conv_general_dilated(
        fields,
        grads_all,
        (1, 1),
        "VALID",
        dimension_numbers=("CHWN", "IHWO", "HWNC"),
        preferred_element_type=jnp.float32,
    )
    parts = lax.axis_size("rk")
    partial = partial.reshape(3, 3, parts, width // parts, out_width).transpose(2, 0, 1, 3, 4)
    return reduce_chunks(partial, "rk", jnp.bfloat16)


def make_body(groups, row_devices):
    def on_device(
        latent,
        stale_latent,
        stale_hidden,
        first_kernel,
        second_kernel,
        scale_table,
        timestep,
        cotangent,
    ):
        row_index = lax.axis_index(ROWS)
        height = latent.shape[0] * row_devices
        latent_f = latent.astype(jnp.float32)
        act = jax.nn.silu(latent_f).astype(jnp.bfloat16)
        edge_act = jax.nn.silu(stale_latent.astype(jnp.float32)).astype(jnp.bfloat16)
        def gathered(field, edges):
            joined = jnp.concatenate([edges[0:1], field, edges[1:2]], axis=0)
            joined = lax.all_gather(joined, CHAN, axis=2, tiled=True)
            rows = field.shape[0]
            above = jnp.where(row_index > 0, joined[0:1], jnp.zeros_like(joined[0:1]))
            below = jnp.where(row_index < row_devices - 1, joined[rows + 1 :], jnp.zeros_like(joined[0:1]))
            middle = joined[1 : rows + 1]
            return middle, jnp.concatenate([above, middle, below], axis=0)

        def pair_reduce(chunks, axis):
            mine = lax.axis_index(axis)
            keep = jnp.where(mine == 0, chunks[0], chunks[1])
            give = jnp.where(mine == 0, chunks[1], chunks[0])
            return keep + lax.ppermute(give, axis, [(0, 1), (1, 0)])

        def chan_reduce(values):
            rows, cols, width = values.shape
            outer, inner = lax.axis_size("cx"), lax.axis_size("cc")
            chunks = values.reshape(rows, cols, outer, inner, width // (outer * inner))
            chunks = chunks.transpose(3, 2, 0, 1, 4)
            return pair_reduce(pair_reduce(chunks, "cc"), "cx")

        act_all, act_pad = gathered(act, edge_act)
        pre_act = conv_rows(act_pad, first_kernel)
        steps_iota = jnp.arange(scale_table.shape[0])[:, None]
        step_scale = jnp.sum(jnp.where(steps_iota == timestep[0], scale_table, 0.0), axis=0)
        scaled = pre_act * step_scale
        hidden = jax.nn.silu(scaled).astype(jnp.bfloat16)
        hidden_all, hidden_pad = gathered(hidden, stale_hidden)
        output = (latent_f + conv_rows(hidden_pad, second_kernel)).astype(jnp.bfloat16)
        grad_pad = extended(cotangent, ROWS, row_devices, 0, 1)
        grad_hidden = chan_reduce(conv_rows(grad_pad, flipped(second_kernel)))
        delta = (grad_hidden * silu_slope(scaled) * step_scale).astype(jnp.bfloat16)
        delta_pad = extended(delta, ROWS, row_devices, 0, 1)
        grad_pre = chan_reduce(conv_rows(delta_pad, flipped(first_kernel)))
        grad_latent = (
            latent_f * 0.0 + cotangent.astype(jnp.float32) + grad_pre * silu_slope(latent_f)
        ).astype(jnp.bfloat16)
        rim_fields = extended(jnp.stack((act_all, hidden_all)), ROWS, row_devices, 1, 1)
        grad_second = weight_grad(rim_fields[1], cotangent, groups) / height
        grad_first = weight_grad(rim_fields[0], delta, groups) / height
        return (output, grad_latent, grad_first, grad_second)

    return on_device


def solution(mesh):
    row_devices, chan_devices = mesh.devices.shape
    groups = 4
    sub = Mesh(
        mesh.devices.reshape(groups, row_devices // groups, 2, chan_devices // 2), ("ry", "rk", "cx", "cc")
    )
    rows_spec = P(ROWS, None, CHAN)
    in_specs = (
        rows_spec,
        rows_spec,
        rows_spec,
        P(None, None, None, CHAN),
        P(None, None, None, CHAN),
        P(None, CHAN),
        P(),
        rows_spec,
    )
    out_specs = (
        rows_spec,
        rows_spec,
        P(None, None, ROWS, CHAN),
        P(None, None, ROWS, CHAN),
    )
    return jax.shard_map(
        make_body(groups, row_devices), mesh=sub, in_specs=in_specs, out_specs=out_specs, check_vma=False
    )
```

```python
import jax
import jax.numpy as jnp
from jax import lax
from jax.sharding import Mesh
from jax.sharding import PartitionSpec as P

ROWS = ("ry", "rk")
CHAN = ("cx", "cc")


def extended(shard, axis, peers, dim, width):
    length = shard.shape[dim]
    up = [(i, (i + 1) % peers) for i in range(peers - 1)]
    down = [(j, i) for i, j in up]
    last = lax.slice_in_dim(shard, length - width, length, axis=dim)
    leading = lax.slice_in_dim(shard, 0, width, axis=dim)
    before = lax.ppermute(last, axis, up)
    after = lax.ppermute(leading, axis, down)
    return jnp.concatenate([before, shard, after], axis=dim)


def silu_slope(values):
    logistic = jax.nn.sigmoid(values)
    return logistic * (1.0 + values * (1.0 - logistic))


def conv_rows(padded, kernel):
    result = lax.conv_general_dilated(
        padded[None],
        kernel,
        (1, 1),
        ((0, 0), (1, 1)),
        dimension_numbers=("NHWC", "HWIO", "NHWC"),
        preferred_element_type=jnp.float32,
    )
    return result[0]


def flipped(kernel):
    return jnp.transpose(kernel[::-1, ::-1], (0, 1, 3, 2))


def shift_exchange(chunks, axis, n, gather=False):
    me = lax.axis_index(axis)
    own = chunks if gather else lax.dynamic_index_in_dim(chunks, me, 0, keepdims=False)
    got = [own]
    for shift in range(1, n):
        piece = chunks if gather else lax.dynamic_index_in_dim(chunks, (me + shift) % n, 0, keepdims=False)
        got.append(lax.ppermute(piece, axis, [(i, (i + shift) % n) for i in range(n)]))
    return jnp.stack(got)


def weight_grad(field_ext, grads, groups):
    rows, cols, out_width = grads.shape
    width = field_ext.shape[2] // groups
    pieces = field_ext.reshape(rows + 2, cols, groups, width).transpose(2, 0, 1, 3)
    fields = shift_exchange(pieces, "ry", groups)
    fields = jnp.pad(fields, ((0, 0), (0, 0), (1, 1), (0, 0)))
    grads_all = shift_exchange(grads, "ry", groups, gather=True)
    partial = lax.conv_general_dilated(
        fields,
        grads_all,
        (1, 1),
        "VALID",
        dimension_numbers=("CHWN", "IHWO", "HWNC"),
        preferred_element_type=jnp.float32,
    )
    parts = lax.axis_size("rk")
    partial = partial.reshape(3, 3, parts, width // parts, out_width).transpose(2, 0, 1, 3, 4)
    received = shift_exchange(partial.astype(jnp.bfloat16), "rk", parts)
    return jnp.sum(received.astype(jnp.float32), axis=0)


def make_body(groups, row_devices):
    def on_device(
        latent,
        stale_latent,
        stale_hidden,
        first_kernel,
        second_kernel,
        scale_table,
        timestep,
        cotangent,
    ):
        row_index = lax.axis_index(ROWS)
        height = latent.shape[0] * row_devices
        latent_f = latent.astype(jnp.float32)
        act = jax.nn.silu(latent_f).astype(jnp.bfloat16)
        edge_act = jax.nn.silu(stale_latent.astype(jnp.float32)).astype(jnp.bfloat16)
        def gathered(field, edges):
            joined = jnp.concatenate([edges[0:1], field, edges[1:2]], axis=0)
            joined = lax.all_gather(joined, CHAN, axis=2, tiled=True)
            rows = field.shape[0]
            above = jnp.where(row_index > 0, joined[0:1], jnp.zeros_like(joined[0:1]))
            below = jnp.where(row_index < row_devices - 1, joined[rows + 1 :], jnp.zeros_like(joined[0:1]))
            middle = joined[1 : rows + 1]
            return middle, jnp.concatenate([above, middle, below], axis=0)

        def pair_reduce(chunks, axis):
            mine = lax.axis_index(axis)
            keep = jnp.where(mine == 0, chunks[0], chunks[1])
            give = jnp.where(mine == 0, chunks[1], chunks[0])
            return keep + lax.ppermute(give, axis, [(0, 1), (1, 0)])

        def chan_reduce(values):
            rows, cols, width = values.shape
            outer, inner = lax.axis_size("cx"), lax.axis_size("cc")
            chunks = values.reshape(rows, cols, outer, inner, width // (outer * inner))
            chunks = chunks.transpose(3, 2, 0, 1, 4)
            return pair_reduce(pair_reduce(chunks, "cc"), "cx")

        act_all, act_pad = gathered(act, edge_act)
        pre_act = conv_rows(act_pad, first_kernel)
        steps_iota = jnp.arange(scale_table.shape[0])[:, None]
        step_scale = jnp.sum(jnp.where(steps_iota == timestep[0], scale_table, 0.0), axis=0)
        scaled = pre_act * step_scale
        hidden = jax.nn.silu(scaled).astype(jnp.bfloat16)
        hidden_all, hidden_pad = gathered(hidden, stale_hidden)
        output = (latent_f + conv_rows(hidden_pad, second_kernel)).astype(jnp.bfloat16)
        grad_pad = extended(cotangent, ROWS, row_devices, 0, 1)
        grad_hidden = chan_reduce(conv_rows(grad_pad, flipped(second_kernel)))
        delta = (grad_hidden * silu_slope(scaled) * step_scale).astype(jnp.bfloat16)
        delta_pad = extended(delta, ROWS, row_devices, 0, 1)
        grad_pre = chan_reduce(conv_rows(delta_pad, flipped(first_kernel)))
        grad_latent = (
            latent_f * 0.0 + cotangent.astype(jnp.float32) + grad_pre * silu_slope(latent_f)
        ).astype(jnp.bfloat16)
        rim_fields = extended(jnp.stack((act_all, hidden_all)), ROWS, row_devices, 1, 1)
        grad_second = weight_grad(rim_fields[1], cotangent, groups) / height
        grad_first = weight_grad(rim_fields[0], delta, groups) / height
        return (output, grad_latent, grad_first, grad_second)

    return on_device


def solution(mesh):
    row_devices, chan_devices = mesh.devices.shape
    groups = 4
    sub = Mesh(
        mesh.devices.reshape(groups, row_devices // groups, 2, chan_devices // 2), ("ry", "rk", "cx", "cc")
    )
    rows_spec = P(ROWS, None, CHAN)
    in_specs = (
        rows_spec,
        rows_spec,
        rows_spec,
        P(None, None, None, CHAN),
        P(None, None, None, CHAN),
        P(None, CHAN),
        P(),
        rows_spec,
    )
    out_specs = (
        rows_spec,
        rows_spec,
        P(None, None, ROWS, CHAN),
        P(None, None, ROWS, CHAN),
    )
    return jax.shard_map(
        make_body(groups, row_devices), mesh=sub, in_specs=in_specs, out_specs=out_specs, check_vma=False
    )
```

```python
import jax
import jax.numpy as jnp
from jax import lax
from jax.sharding import Mesh
from jax.sharding import PartitionSpec as P

ROWS = ("ry", "rk")
CHAN = ("cx", "cc")


def extended(shard, axis, peers, dim, width):
    length = shard.shape[dim]
    up = [(i, (i + 1) % peers) for i in range(peers - 1)]
    down = [(j, i) for i, j in up]
    last = lax.slice_in_dim(shard, length - width, length, axis=dim)
    leading = lax.slice_in_dim(shard, 0, width, axis=dim)
    before = lax.ppermute(last, axis, up)
    after = lax.ppermute(leading, axis, down)
    return jnp.concatenate([before, shard, after], axis=dim)


def silu_slope(values):
    logistic = jax.nn.sigmoid(values)
    return logistic * (1.0 + values * (1.0 - logistic))


def conv_rows(padded, kernel):
    result = lax.conv_general_dilated(
        padded[None],
        kernel,
        (1, 1),
        ((0, 0), (1, 1)),
        dimension_numbers=("NHWC", "HWIO", "NHWC"),
        preferred_element_type=jnp.float32,
    )
    return result[0]


def flipped(kernel):
    return jnp.transpose(kernel[::-1, ::-1], (0, 1, 3, 2))


def reduce_chunks(chunks, axis, link_type=jnp.float32):
    received = lax.all_to_all(chunks.astype(link_type), axis, 0, 0, tiled=True)
    return jnp.sum(received.astype(jnp.float32), axis=0)


def weight_grad(field_ext, grads, groups):
    rows, cols, out_width = grads.shape
    width = field_ext.shape[2] // groups
    pieces = field_ext.reshape(rows + 2, cols, groups, width).transpose(2, 0, 1, 3)
    fields = lax.all_to_all(pieces, "ry", 0, 0, tiled=True)
    fields = jnp.pad(fields, ((0, 0), (0, 0), (1, 1), (0, 0)))
    grads_all = lax.all_gather(grads, "ry", axis=0, tiled=False)
    partial = lax.conv_general_dilated(
        fields,
        grads_all,
        (1, 1),
        "VALID",
        dimension_numbers=("CHWN", "IHWO", "HWNC"),
        preferred_element_type=jnp.float32,
    )
    parts = lax.axis_size("rk")
    partial = partial.reshape(3, 3, parts, width // parts, out_width).transpose(2, 0, 1, 3, 4)
    return reduce_chunks(partial, "rk", jnp.bfloat16)


def make_body(groups, row_devices):
    def on_device(
        latent,
        stale_latent,
        stale_hidden,
        first_kernel,
        second_kernel,
        scale_table,
        timestep,
        cotangent,
    ):
        row_index = lax.axis_index(ROWS)
        height = latent.shape[0] * row_devices
        latent_f = latent.astype(jnp.float32)
        act = jax.nn.silu(latent_f).astype(jnp.bfloat16)
        edge_act = jax.nn.silu(stale_latent.astype(jnp.float32)).astype(jnp.bfloat16)
        def gathered(field, edges):
            joined = jnp.concatenate([edges[0:1], field, edges[1:2]], axis=0)
            joined = pair_gather(pair_gather(joined, "cc"), "cx")
            rows = field.shape[0]
            above = jnp.where(row_index > 0, joined[0:1], jnp.zeros_like(joined[0:1]))
            below = jnp.where(row_index < row_devices - 1, joined[rows + 1 :], jnp.zeros_like(joined[0:1]))
            middle = joined[1 : rows + 1]
            return middle, jnp.concatenate([above, middle, below], axis=0)

        def pair_gather(part, axis):
            other = lax.ppermute(part, axis, [(0, 1), (1, 0)])
            first = lax.axis_index(axis) == 0
            return jnp.concatenate([jnp.where(first, part, other), jnp.where(first, other, part)], axis=2)

        def pair_reduce(chunks, axis):
            mine = lax.axis_index(axis)
            keep = jnp.where(mine == 0, chunks[0], chunks[1])
            give = jnp.where(mine == 0, chunks[1], chunks[0])
            return keep + lax.ppermute(give, axis, [(0, 1), (1, 0)])

        def chan_reduce(values):
            rows, cols, width = values.shape
            outer, inner = lax.axis_size("cx"), lax.axis_size("cc")
            chunks = values.reshape(rows, cols, outer, inner, width // (outer * inner))
            chunks = chunks.transpose(3, 2, 0, 1, 4)
            return pair_reduce(pair_reduce(chunks, "cc"), "cx")

        act_all, act_pad = gathered(act, edge_act)
        pre_act = conv_rows(act_pad, first_kernel)
        steps_iota = jnp.arange(scale_table.shape[0])[:, None]
        step_scale = jnp.sum(jnp.where(steps_iota == timestep[0], scale_table, 0.0), axis=0)
        scaled = pre_act * step_scale
        hidden = jax.nn.silu(scaled).astype(jnp.bfloat16)
        hidden_all, hidden_pad = gathered(hidden, stale_hidden)
        output = (latent_f + conv_rows(hidden_pad, second_kernel)).astype(jnp.bfloat16)
        grad_pad = extended(cotangent, ROWS, row_devices, 0, 1)
        grad_hidden = chan_reduce(conv_rows(grad_pad, flipped(second_kernel)))
        delta = (grad_hidden * silu_slope(scaled) * step_scale).astype(jnp.bfloat16)
        delta_pad = extended(delta, ROWS, row_devices, 0, 1)
        grad_pre = chan_reduce(conv_rows(delta_pad, flipped(first_kernel)))
        grad_latent = (
            latent_f * 0.0 + cotangent.astype(jnp.float32) + grad_pre * silu_slope(latent_f)
        ).astype(jnp.bfloat16)
        rim_fields = extended(jnp.stack((act_all, hidden_all)), ROWS, row_devices, 1, 1)
        grad_second = weight_grad(rim_fields[1], cotangent, groups) / height
        grad_first = weight_grad(rim_fields[0], delta, groups) / height
        return (output, grad_latent, grad_first, grad_second)

    return on_device


def solution(mesh):
    row_devices, chan_devices = mesh.devices.shape
    groups = 4
    sub = Mesh(
        mesh.devices.reshape(groups, row_devices // groups, 2, chan_devices // 2), ("ry", "rk", "cx", "cc")
    )
    rows_spec = P(ROWS, None, CHAN)
    in_specs = (
        rows_spec,
        rows_spec,
        rows_spec,
        P(None, None, None, CHAN),
        P(None, None, None, CHAN),
        P(None, CHAN),
        P(),
        rows_spec,
    )
    out_specs = (
        rows_spec,
        rows_spec,
        P(None, None, ROWS, CHAN),
        P(None, None, ROWS, CHAN),
    )
    return jax.shard_map(
        make_body(groups, row_devices), mesh=sub, in_specs=in_specs, out_specs=out_specs, check_vma=False
    )
```

```python
import jax
import jax.numpy as jnp
from jax import lax
from jax.sharding import Mesh
from jax.sharding import PartitionSpec as P

ROWS = ("ry", "rk")
CHAN = ("cx", "cc")


def extended(shard, axis, peers, dim, width):
    length = shard.shape[dim]
    up = [(i, (i + 1) % peers) for i in range(peers - 1)]
    down = [(j, i) for i, j in up]
    last = lax.slice_in_dim(shard, length - width, length, axis=dim)
    leading = lax.slice_in_dim(shard, 0, width, axis=dim)
    before = lax.ppermute(last, axis, up)
    after = lax.ppermute(leading, axis, down)
    return jnp.concatenate([before, shard, after], axis=dim)


def silu_slope(values):
    logistic = jax.nn.sigmoid(values)
    return logistic * (1.0 + values * (1.0 - logistic))


def conv_rows(padded, kernel):
    result = lax.conv_general_dilated(
        padded[None],
        kernel,
        (1, 1),
        ((0, 0), (1, 1)),
        dimension_numbers=("NHWC", "HWIO", "NHWC"),
        preferred_element_type=jnp.float32,
    )
    return result[0]


def flipped(kernel):
    return jnp.transpose(kernel[::-1, ::-1], (0, 1, 3, 2))


def reduce_chunks(chunks, axis, link_type=jnp.float32):
    received = lax.all_to_all(chunks.astype(link_type), axis, 0, 0, tiled=True)
    return jnp.sum(received.astype(jnp.float32), axis=0)


def weight_grad(field_ext, grads, groups, grads_all=None):
    rows, cols, out_width = grads.shape
    width = field_ext.shape[2] // groups
    pieces = field_ext.reshape(rows + 2, cols, groups, width).transpose(2, 0, 1, 3)
    fields = lax.all_to_all(pieces, "ry", 0, 0, tiled=True)
    fields = jnp.pad(fields, ((0, 0), (0, 0), (1, 1), (0, 0)))
    if grads_all is None:
        grads_all = lax.all_gather(grads, "ry", axis=0, tiled=False)
    partial = lax.conv_general_dilated(
        fields,
        grads_all,
        (1, 1),
        "VALID",
        dimension_numbers=("CHWN", "IHWO", "HWNC"),
        preferred_element_type=jnp.float32,
    )
    parts = lax.axis_size("rk")
    partial = partial.reshape(3, 3, parts, width // parts, out_width).transpose(2, 0, 1, 3, 4)
    return reduce_chunks(partial, "rk", jnp.bfloat16)


def make_body(groups, row_devices):
    def on_device(
        latent,
        stale_latent,
        stale_hidden,
        first_kernel,
        second_kernel,
        scale_table,
        timestep,
        cotangent,
    ):
        row_index = lax.axis_index(ROWS)
        height = latent.shape[0] * row_devices
        latent_f = latent.astype(jnp.float32)
        act = jax.nn.silu(latent_f).astype(jnp.bfloat16)
        edge_act = jax.nn.silu(stale_latent.astype(jnp.float32)).astype(jnp.bfloat16)
        def gathered(field, edges):
            joined = jnp.concatenate([edges[0:1], field, edges[1:2]], axis=0)
            joined = lax.all_gather(joined, CHAN, axis=2, tiled=True)
            rows = field.shape[0]
            above = jnp.where(row_index > 0, joined[0:1], jnp.zeros_like(joined[0:1]))
            below = jnp.where(row_index < row_devices - 1, joined[rows + 1 :], jnp.zeros_like(joined[0:1]))
            middle = joined[1 : rows + 1]
            return middle, jnp.concatenate([above, middle, below], axis=0)

        def pair_reduce(chunks, axis):
            mine = lax.axis_index(axis)
            keep = jnp.where(mine == 0, chunks[0], chunks[1])
            give = jnp.where(mine == 0, chunks[1], chunks[0])
            return keep + lax.ppermute(give, axis, [(0, 1), (1, 0)])

        def chan_reduce(values):
            rows, cols, width = values.shape
            outer, inner = lax.axis_size("cx"), lax.axis_size("cc")
            chunks = values.reshape(rows, cols, outer, inner, width // (outer * inner))
            chunks = chunks.transpose(3, 2, 0, 1, 4)
            return pair_reduce(pair_reduce(chunks, "cc"), "cx")

        act_all, act_pad = gathered(act, edge_act)
        pre_act = conv_rows(act_pad, first_kernel)
        steps_iota = jnp.arange(scale_table.shape[0])[:, None]
        step_scale = jnp.sum(jnp.where(steps_iota == timestep[0], scale_table, 0.0), axis=0)
        scaled = pre_act * step_scale
        hidden = jax.nn.silu(scaled).astype(jnp.bfloat16)
        hidden_all, hidden_pad = gathered(hidden, stale_hidden)
        output = (latent_f + conv_rows(hidden_pad, second_kernel)).astype(jnp.bfloat16)
        cot_rows = lax.all_to_all(
            jnp.broadcast_to(cotangent[None], (groups,) + cotangent.shape), "ry", 0, 0, tiled=True
        )
        cot_rows, cot_held = lax.optimization_barrier((cot_rows, cotangent))
        grad_pad = extended(cot_held, ROWS, row_devices, 0, 1)
        grad_hidden = chan_reduce(conv_rows(grad_pad, flipped(second_kernel)))
        delta = (grad_hidden * silu_slope(scaled) * step_scale).astype(jnp.bfloat16)
        delta_pad = extended(delta, ROWS, row_devices, 0, 1)
        grad_pre = chan_reduce(conv_rows(delta_pad, flipped(first_kernel)))
        grad_latent = (
            latent_f * 0.0 + cotangent.astype(jnp.float32) + grad_pre * silu_slope(latent_f)
        ).astype(jnp.bfloat16)
        rim_fields = extended(jnp.stack((act_all, hidden_all)), ROWS, row_devices, 1, 1)
        grad_second = weight_grad(rim_fields[1], cotangent, groups, cot_rows) / height
        grad_first = weight_grad(rim_fields[0], delta, groups) / height
        return (output, grad_latent, grad_first, grad_second)

    return on_device


def solution(mesh):
    row_devices, chan_devices = mesh.devices.shape
    groups = 4
    sub = Mesh(
        mesh.devices.reshape(groups, row_devices // groups, 2, chan_devices // 2), ("ry", "rk", "cx", "cc")
    )
    rows_spec = P(ROWS, None, CHAN)
    in_specs = (
        rows_spec,
        rows_spec,
        rows_spec,
        P(None, None, None, CHAN),
        P(None, None, None, CHAN),
        P(None, CHAN),
        P(),
        rows_spec,
    )
    out_specs = (
        rows_spec,
        rows_spec,
        P(None, None, ROWS, CHAN),
        P(None, None, ROWS, CHAN),
    )
    return jax.shard_map(
        make_body(groups, row_devices), mesh=sub, in_specs=in_specs, out_specs=out_specs, check_vma=False
    )
```

```python
import jax
import jax.numpy as jnp
from jax import lax
from jax.sharding import Mesh
from jax.sharding import PartitionSpec as P

ROWS = ("ry", "rk")
CHAN = ("cx", "cc")


def extended(shard, axis, peers, dim, width):
    length = shard.shape[dim]
    up = [(i, (i + 1) % peers) for i in range(peers - 1)]
    down = [(j, i) for i, j in up]
    last = lax.slice_in_dim(shard, length - width, length, axis=dim)
    leading = lax.slice_in_dim(shard, 0, width, axis=dim)
    before = lax.ppermute(last, axis, up)
    after = lax.ppermute(leading, axis, down)
    return jnp.concatenate([before, shard, after], axis=dim)


def silu_slope(values):
    logistic = jax.nn.sigmoid(values)
    return logistic * (1.0 + values * (1.0 - logistic))


def conv_rows(padded, kernel):
    result = lax.conv_general_dilated(
        padded[None],
        kernel,
        (1, 1),
        ((0, 0), (1, 1)),
        dimension_numbers=("NHWC", "HWIO", "NHWC"),
        preferred_element_type=jnp.float32,
    )
    return result[0]


def flipped(kernel):
    return jnp.transpose(kernel[::-1, ::-1], (0, 1, 3, 2))


def reduce_chunks(chunks, axis, link_type=jnp.float32):
    received = lax.all_to_all(chunks.astype(link_type), axis, 0, 0, tiled=True)
    return jnp.sum(received.astype(jnp.float32), axis=0)


def weight_grad(field_ext, grads, groups, grads_all=None):
    rows, cols, out_width = grads.shape
    width = field_ext.shape[2] // groups
    pieces = field_ext.reshape(rows + 2, cols, groups, width).transpose(2, 0, 1, 3)
    fields = lax.all_to_all(pieces, "ry", 0, 0, tiled=True)
    fields = jnp.pad(fields, ((0, 0), (0, 0), (1, 1), (0, 0)))
    if grads_all is None:
        grads_all = lax.all_gather(grads, "ry", axis=0, tiled=False)
    partial = lax.conv_general_dilated(
        fields,
        grads_all,
        (1, 1),
        "VALID",
        dimension_numbers=("CHWN", "IHWO", "HWNC"),
        preferred_element_type=jnp.float32,
    )
    parts = lax.axis_size("rk")
    partial = partial.reshape(3, 3, parts, width // parts, out_width).transpose(2, 0, 1, 3, 4)
    return reduce_chunks(partial, "rk", jnp.bfloat16)


def make_body(groups, row_devices):
    def on_device(
        latent,
        stale_latent,
        stale_hidden,
        first_kernel,
        second_kernel,
        scale_table,
        timestep,
        cotangent,
    ):
        row_index = lax.axis_index(ROWS)
        height = latent.shape[0] * row_devices
        latent_f = latent.astype(jnp.float32)
        act = jax.nn.silu(latent_f).astype(jnp.bfloat16)
        edge_act = jax.nn.silu(stale_latent.astype(jnp.float32)).astype(jnp.bfloat16)
        def gathered(field, edges):
            joined = jnp.concatenate([edges[0:1], field, edges[1:2]], axis=0)
            joined = lax.all_gather(joined, CHAN, axis=2, tiled=True)
            rows = field.shape[0]
            above = jnp.where(row_index > 0, joined[0:1], jnp.zeros_like(joined[0:1]))
            below = jnp.where(row_index < row_devices - 1, joined[rows + 1 :], jnp.zeros_like(joined[0:1]))
            middle = joined[1 : rows + 1]
            return middle, jnp.concatenate([above, middle, below], axis=0)

        def pair_reduce(chunks, axis):
            mine = lax.axis_index(axis)
            keep = jnp.where(mine == 0, chunks[0], chunks[1])
            give = jnp.where(mine == 0, chunks[1], chunks[0])
            return keep + lax.ppermute(give, axis, [(0, 1), (1, 0)])

        def chan_reduce(values):
            rows, cols, width = values.shape
            outer, inner = lax.axis_size("cx"), lax.axis_size("cc")
            chunks = values.reshape(rows, cols, outer, inner, width // (outer * inner))
            chunks = chunks.transpose(3, 2, 0, 1, 4)
            return pair_reduce(pair_reduce(chunks, "cc"), "cx")

        act_all, act_pad = gathered(act, edge_act)
        cot_rows = lax.all_to_all(
            jnp.broadcast_to(cotangent[None], (groups,) + cotangent.shape), "ry", 0, 0, tiled=True
        )
        pre_act = conv_rows(act_pad, first_kernel)
        cot_rows, pre_act = lax.optimization_barrier((cot_rows, pre_act))
        steps_iota = jnp.arange(scale_table.shape[0])[:, None]
        step_scale = jnp.sum(jnp.where(steps_iota == timestep[0], scale_table, 0.0), axis=0)
        scaled = pre_act * step_scale
        hidden = jax.nn.silu(scaled).astype(jnp.bfloat16)
        hidden_all, hidden_pad = gathered(hidden, stale_hidden)
        output = (latent_f + conv_rows(hidden_pad, second_kernel)).astype(jnp.bfloat16)
        grad_pad = extended(cotangent, ROWS, row_devices, 0, 1)
        grad_hidden = chan_reduce(conv_rows(grad_pad, flipped(second_kernel)))
        delta = (grad_hidden * silu_slope(scaled) * step_scale).astype(jnp.bfloat16)
        delta_pad = extended(delta, ROWS, row_devices, 0, 1)
        grad_pre = chan_reduce(conv_rows(delta_pad, flipped(first_kernel)))
        grad_latent = (
            latent_f * 0.0 + cotangent.astype(jnp.float32) + grad_pre * silu_slope(latent_f)
        ).astype(jnp.bfloat16)
        rim_fields = extended(jnp.stack((act_all, hidden_all)), ROWS, row_devices, 1, 1)
        grad_second = weight_grad(rim_fields[1], cotangent, groups, cot_rows) / height
        grad_first = weight_grad(rim_fields[0], delta, groups) / height
        return (output, grad_latent, grad_first, grad_second)

    return on_device


def solution(mesh):
    row_devices, chan_devices = mesh.devices.shape
    groups = 4
    sub = Mesh(
        mesh.devices.reshape(groups, row_devices // groups, 2, chan_devices // 2), ("ry", "rk", "cx", "cc")
    )
    rows_spec = P(ROWS, None, CHAN)
    in_specs = (
        rows_spec,
        rows_spec,
        rows_spec,
        P(None, None, None, CHAN),
        P(None, None, None, CHAN),
        P(None, CHAN),
        P(),
        rows_spec,
    )
    out_specs = (
        rows_spec,
        rows_spec,
        P(None, None, ROWS, CHAN),
        P(None, None, ROWS, CHAN),
    )
    return jax.shard_map(
        make_body(groups, row_devices), mesh=sub, in_specs=in_specs, out_specs=out_specs, check_vma=False
    )
```

```python
import jax
import jax.numpy as jnp
from jax import lax
from jax.sharding import Mesh
from jax.sharding import PartitionSpec as P

ROWS = ("ry", "rk")
CHAN = ("cx", "cc")


def extended(shard, axis, peers, dim, width):
    length = shard.shape[dim]
    up = [(i, (i + 1) % peers) for i in range(peers - 1)]
    down = [(j, i) for i, j in up]
    last = lax.slice_in_dim(shard, length - width, length, axis=dim)
    leading = lax.slice_in_dim(shard, 0, width, axis=dim)
    before = lax.ppermute(last, axis, up)
    after = lax.ppermute(leading, axis, down)
    return jnp.concatenate([before, shard, after], axis=dim)


def silu_slope(values):
    logistic = jax.nn.sigmoid(values)
    return logistic * (1.0 + values * (1.0 - logistic))


def conv_rows(padded, kernel):
    result = lax.conv_general_dilated(
        padded[None],
        kernel,
        (1, 1),
        ((0, 0), (1, 1)),
        dimension_numbers=("NHWC", "HWIO", "NHWC"),
        preferred_element_type=jnp.float32,
    )
    return result[0]


def flipped(kernel):
    return jnp.transpose(kernel[::-1, ::-1], (0, 1, 3, 2))


def reduce_chunks(chunks, axis, link_type=jnp.float32):
    received = lax.all_to_all(chunks.astype(link_type), axis, 0, 0, tiled=True)
    return jnp.sum(received.astype(jnp.float32), axis=0)


def row_fields(field_ext, groups):
    rows, cols, channels = field_ext.shape
    pieces = field_ext.reshape(rows, cols, groups, channels // groups).transpose(2, 0, 1, 3)
    fields = lax.all_to_all(pieces, "ry", 0, 0, tiled=True)
    return jnp.pad(fields, ((0, 0), (0, 0), (1, 1), (0, 0)))


def weight_grad(fields, grads, groups, grads_all=None):
    rows, cols, out_width = grads.shape
    width = fields.shape[3]
    if grads_all is None:
        grads_all = lax.all_gather(grads, "ry", axis=0, tiled=False)
    partial = lax.conv_general_dilated(
        fields,
        grads_all,
        (1, 1),
        "VALID",
        dimension_numbers=("CHWN", "IHWO", "HWNC"),
        preferred_element_type=jnp.float32,
    )
    parts = lax.axis_size("rk")
    partial = partial.reshape(3, 3, parts, width // parts, out_width).transpose(2, 0, 1, 3, 4)
    return reduce_chunks(partial, "rk", jnp.bfloat16)


def make_body(groups, row_devices):
    def on_device(
        latent,
        stale_latent,
        stale_hidden,
        first_kernel,
        second_kernel,
        scale_table,
        timestep,
        cotangent,
    ):
        row_index = lax.axis_index(ROWS)
        height = latent.shape[0] * row_devices
        latent_f = latent.astype(jnp.float32)
        act = jax.nn.silu(latent_f).astype(jnp.bfloat16)
        edge_act = jax.nn.silu(stale_latent.astype(jnp.float32)).astype(jnp.bfloat16)
        def gathered(field, edges):
            joined = jnp.concatenate([edges[0:1], field, edges[1:2]], axis=0)
            joined = lax.all_gather(joined, CHAN, axis=2, tiled=True)
            rows = field.shape[0]
            above = jnp.where(row_index > 0, joined[0:1], jnp.zeros_like(joined[0:1]))
            below = jnp.where(row_index < row_devices - 1, joined[rows + 1 :], jnp.zeros_like(joined[0:1]))
            middle = joined[1 : rows + 1]
            return middle, jnp.concatenate([above, middle, below], axis=0)

        def pair_reduce(chunks, axis):
            mine = lax.axis_index(axis)
            keep = jnp.where(mine == 0, chunks[0], chunks[1])
            give = jnp.where(mine == 0, chunks[1], chunks[0])
            return keep + lax.ppermute(give, axis, [(0, 1), (1, 0)])

        def chan_reduce(values):
            rows, cols, width = values.shape
            outer, inner = lax.axis_size("cx"), lax.axis_size("cc")
            chunks = values.reshape(rows, cols, outer, inner, width // (outer * inner))
            chunks = chunks.transpose(3, 2, 0, 1, 4)
            return pair_reduce(pair_reduce(chunks, "cc"), "cx")

        act_all, act_pad = gathered(act, edge_act)
        act_fields = row_fields(extended(act_all, ROWS, row_devices, 0, 1), groups)
        cot_rows = lax.all_to_all(
            jnp.broadcast_to(cotangent[None], (groups,) + cotangent.shape), "ry", 0, 0, tiled=True
        )
        pre_act = conv_rows(act_pad, first_kernel)
        cot_rows, pre_act = lax.optimization_barrier((cot_rows, pre_act))
        steps_iota = jnp.arange(scale_table.shape[0])[:, None]
        step_scale = jnp.sum(jnp.where(steps_iota == timestep[0], scale_table, 0.0), axis=0)
        scaled = pre_act * step_scale
        hidden = jax.nn.silu(scaled).astype(jnp.bfloat16)
        hidden_all, hidden_pad = gathered(hidden, stale_hidden)
        output = (latent_f + conv_rows(hidden_pad, second_kernel)).astype(jnp.bfloat16)
        grad_pad = extended(cotangent, ROWS, row_devices, 0, 1)
        grad_hidden = chan_reduce(conv_rows(grad_pad, flipped(second_kernel)))
        delta = (grad_hidden * silu_slope(scaled) * step_scale).astype(jnp.bfloat16)
        act_fields, delta = lax.optimization_barrier((act_fields, delta))
        delta_pad = extended(delta, ROWS, row_devices, 0, 1)
        grad_pre = chan_reduce(conv_rows(delta_pad, flipped(first_kernel)))
        grad_latent = (
            latent_f * 0.0 + cotangent.astype(jnp.float32) + grad_pre * silu_slope(latent_f)
        ).astype(jnp.bfloat16)
        hidden_fields = row_fields(extended(hidden_all, ROWS, row_devices, 0, 1), groups)
        grad_second = weight_grad(hidden_fields, cotangent, groups, cot_rows) / height
        grad_first = weight_grad(act_fields, delta, groups) / height
        return (output, grad_latent, grad_first, grad_second)

    return on_device


def solution(mesh):
    row_devices, chan_devices = mesh.devices.shape
    groups = 4
    sub = Mesh(
        mesh.devices.reshape(groups, row_devices // groups, 2, chan_devices // 2), ("ry", "rk", "cx", "cc")
    )
    rows_spec = P(ROWS, None, CHAN)
    in_specs = (
        rows_spec,
        rows_spec,
        rows_spec,
        P(None, None, None, CHAN),
        P(None, None, None, CHAN),
        P(None, CHAN),
        P(),
        rows_spec,
    )
    out_specs = (
        rows_spec,
        rows_spec,
        P(None, None, ROWS, CHAN),
        P(None, None, ROWS, CHAN),
    )
    return jax.shard_map(
        make_body(groups, row_devices), mesh=sub, in_specs=in_specs, out_specs=out_specs, check_vma=False
    )
```

```python
import jax
import jax.numpy as jnp
from jax import lax
from jax.sharding import Mesh
from jax.sharding import PartitionSpec as P

ROWS = ("ry", "rk")
CHAN = ("cx", "cc")


def extended(shard, axis, peers, dim, width):
    length = shard.shape[dim]
    up = [(i, (i + 1) % peers) for i in range(peers - 1)]
    down = [(j, i) for i, j in up]
    last = lax.slice_in_dim(shard, length - width, length, axis=dim)
    leading = lax.slice_in_dim(shard, 0, width, axis=dim)
    before = lax.ppermute(last, axis, up)
    after = lax.ppermute(leading, axis, down)
    return jnp.concatenate([before, shard, after], axis=dim)


def silu_slope(values):
    logistic = jax.nn.sigmoid(values)
    return logistic * (1.0 + values * (1.0 - logistic))


def conv_rows(padded, kernel):
    result = lax.conv_general_dilated(
        padded[None],
        kernel,
        (1, 1),
        ((0, 0), (1, 1)),
        dimension_numbers=("NHWC", "HWIO", "NHWC"),
        preferred_element_type=jnp.float32,
    )
    return result[0]


def flipped(kernel):
    return jnp.transpose(kernel[::-1, ::-1], (0, 1, 3, 2))


def reduce_chunks(chunks, axis, link_type=jnp.float32):
    received = lax.all_to_all(chunks.astype(link_type), axis, 0, 0, tiled=True)
    return jnp.sum(received.astype(jnp.float32), axis=0)


def weight_grad(field_ext, grads, groups, grads_all=None):
    rows, cols, out_width = grads.shape
    width = field_ext.shape[2] // groups
    pieces = field_ext.reshape(rows + 2, cols, groups, width).transpose(2, 0, 1, 3)
    fields = lax.all_to_all(pieces, "ry", 0, 0, tiled=True)
    fields = jnp.pad(fields, ((0, 0), (0, 0), (1, 1), (0, 0)))
    if grads_all is None:
        grads_all = lax.all_gather(grads, "ry", axis=0, tiled=False)
    partial = lax.conv_general_dilated(
        fields,
        grads_all,
        (1, 1),
        "VALID",
        dimension_numbers=("CHWN", "IHWO", "HWNC"),
        preferred_element_type=jnp.float32,
    )
    parts = lax.axis_size("rk")
    partial = partial.reshape(3, 3, parts, width // parts, out_width).transpose(2, 0, 1, 3, 4)
    return reduce_chunks(partial, "rk", jnp.bfloat16)


def make_body(groups, row_devices):
    def on_device(
        latent,
        stale_latent,
        stale_hidden,
        first_kernel,
        second_kernel,
        scale_table,
        timestep,
        cotangent,
    ):
        row_index = lax.axis_index(ROWS)
        height = latent.shape[0] * row_devices
        latent_f = latent.astype(jnp.float32)
        act = jax.nn.silu(latent_f).astype(jnp.bfloat16)
        edge_act = jax.nn.silu(stale_latent.astype(jnp.float32)).astype(jnp.bfloat16)
        def gathered(field, edges):
            joined = jnp.concatenate([edges[0:1], field, edges[1:2]], axis=0)
            joined = lax.all_gather(joined, CHAN, axis=2, tiled=True)
            rows = field.shape[0]
            above = jnp.where(row_index > 0, joined[0:1], jnp.zeros_like(joined[0:1]))
            below = jnp.where(row_index < row_devices - 1, joined[rows + 1 :], jnp.zeros_like(joined[0:1]))
            middle = joined[1 : rows + 1]
            return middle, jnp.concatenate([above, middle, below], axis=0)

        def pair_reduce(chunks, axis):
            mine = lax.axis_index(axis)
            keep = jnp.where(mine == 0, chunks[0], chunks[1])
            give = jnp.where(mine == 0, chunks[1], chunks[0])
            return keep + lax.ppermute(give, axis, [(0, 1), (1, 0)])

        def chan_reduce(values):
            rows, cols, width = values.shape
            outer, inner = lax.axis_size("cx"), lax.axis_size("cc")
            chunks = values.reshape(rows, cols, outer, inner, width // (outer * inner))
            chunks = chunks.transpose(3, 2, 0, 1, 4)
            return pair_reduce(pair_reduce(chunks, "cc"), "cx")

        act_all, act_pad = gathered(act, edge_act)
        cot_rows = lax.all_to_all(
            jnp.broadcast_to(cotangent[None], (groups,) + cotangent.shape), "ry", 0, 0, tiled=True
        )
        pre_act = conv_rows(act_pad, first_kernel)
        steps_iota = jnp.arange(scale_table.shape[0])[:, None]
        step_scale = jnp.sum(jnp.where(steps_iota == timestep[0], scale_table, 0.0), axis=0)
        scaled = pre_act * step_scale
        hidden = jax.nn.silu(scaled).astype(jnp.bfloat16)
        hidden_all, hidden_pad = gathered(hidden, stale_hidden)
        output = (latent_f + conv_rows(hidden_pad, second_kernel)).astype(jnp.bfloat16)
        grad_pad = extended(cotangent, ROWS, row_devices, 0, 1)
        grad_hidden = chan_reduce(conv_rows(grad_pad, flipped(second_kernel)))
        delta = (grad_hidden * silu_slope(scaled) * step_scale).astype(jnp.bfloat16)
        delta_pad = extended(delta, ROWS, row_devices, 0, 1)
        grad_pre = chan_reduce(conv_rows(delta_pad, flipped(first_kernel)))
        grad_latent = (
            latent_f * 0.0 + cotangent.astype(jnp.float32) + grad_pre * silu_slope(latent_f)
        ).astype(jnp.bfloat16)
        rim_fields = extended(jnp.stack((act_all, hidden_all)), ROWS, row_devices, 1, 1)
        grad_second = weight_grad(rim_fields[1], cotangent, groups, cot_rows) / height
        grad_first = weight_grad(rim_fields[0], delta, groups) / height
        return (output, grad_latent, grad_first, grad_second)

    return on_device


def solution(mesh):
    row_devices, chan_devices = mesh.devices.shape
    groups = 4
    sub = Mesh(
        mesh.devices.reshape(groups, row_devices // groups, 2, chan_devices // 2), ("ry", "rk", "cx", "cc")
    )
    rows_spec = P(ROWS, None, CHAN)
    in_specs = (
        rows_spec,
        rows_spec,
        rows_spec,
        P(None, None, None, CHAN),
        P(None, None, None, CHAN),
        P(None, CHAN),
        P(),
        rows_spec,
    )
    out_specs = (
        rows_spec,
        rows_spec,
        P(None, None, ROWS, CHAN),
        P(None, None, ROWS, CHAN),
    )
    return jax.shard_map(
        make_body(groups, row_devices), mesh=sub, in_specs=in_specs, out_specs=out_specs, check_vma=False
    )
```
